128 devices in a mesh: lat: 32 (over x, y, core), dep: 4 (over z).
Axes of the slice: x: 4, y: 4, z: 4, core: 2. Of those that a mesh axis runs over, the one named last changes fastest.
Arguments:
- spectrum: float32 [4, 512, 2, 32768], P('dep', 'lat'), may hold values from -6 to 6
- operator: float32 [2, 2048, 2048], P(None, None, 'dep'), may hold values from -0.125 to 0.125
- pattern: int32 [2, 16, 16], replicated, may hold values 0 or 1
- band: int32 [32768], P('lat'), may hold values from 0 to 1
Outputs:
- blurred: float32 [2048, 2, 32768], P('dep', None, 'lat')
The draws below stay inside these ranges and needn't reach their ends.
All inputs are finite; a program needn't handle non-finite values.
Results may differ from the reference program's by a relative error of at most 0.0001.
Values sent between devices are 32-bit elements; how exact they have to be, the bound alone decides.
No kernel may reach another device: no remote copies, remote signals or barrier semaphores. Data moves between devices by JAX's collectives and lax.ppermute only.
A program may use at most 128 MiB of HBM per device.

```python
import jax
import jax.numpy as jnp
from jax import lax

Z = 2048
BLOCK = 128
BANDS = 2
ZD = 512
ROWS = 32768
NB = 16
N_DEP = 4


def plant(entries, key, smallest, largest):
    place = [jax.random.randint(jax.random.fold_in(key, axis), (), 0, length) for axis, length in enumerate(entries.shape)]
    main_axis = entries.shape.index(max(entries.shape))
    neighbour = place[:main_axis] + [(place[main_axis] + 1) % entries.shape[main_axis]] + place[main_axis + 1:]
    return entries.at[tuple(place)].set(smallest).at[tuple(neighbour)].set(largest)


def level_of(own_key, shape, pieces, least, high):
    loudness = 1.0
    for dim, blocks in pieces:
        draws = jax.random.uniform(jax.random.fold_in(jax.random.fold_in(own_key, 6), dim), (blocks,), jnp.float32, least / len(pieces), high / len(pieces))
        loudness = loudness * jnp.repeat(jnp.exp(draws), shape[dim] // blocks).reshape((-1,) + (1,) * (len(shape) - 1 - dim))
    return loudness


def bell_draw(key, dims, spread, most, split=(), kind=jnp.bfloat16):
    drawn = spread * jax.random.normal(key, dims, jnp.float32)
    if split:
        drawn = drawn * level_of(key, dims, split, -0.22, 0.18)
    return jnp.clip(drawn, -most, most).astype(kind)


def setup_inputs(seed: int = 0) -> dict:
    seeds = jax.random.split(jax.random.key(seed), 5)
    spectrum = bell_draw(seeds[0], (N_DEP, ZD, 2, ROWS), 1.0, 6.0, ((0, 4), (1, 32)), jnp.float32)
    operator = bell_draw(seeds[1], (BANDS, Z, Z), Z ** -0.5, 0.125, ((2, 4),), jnp.float32)
    pattern = plant((jax.random.randint(seeds[2], (BANDS, NB, NB), 0, 3) < 2).astype(jnp.int32), jax.random.fold_in(seeds[2], 1), 0, 1)
    band = plant(jax.random.randint(seeds[3], (ROWS,), 0, BANDS), jax.random.fold_in(seeds[3], 1), 0, BANDS - 1).astype(jnp.int32)
    return dict(spectrum=spectrum, operator=operator, pattern=pattern, band=band)


def reference(spectrum, operator, pattern, band):
    planes = spectrum.reshape(Z, 2 * ROWS)
    field = jnp.repeat(jnp.repeat(pattern, BLOCK, axis=1), BLOCK, axis=2).astype(jnp.float32)
    masked = operator * field
    chosen = (band[None, :] == jnp.arange(BANDS, dtype=jnp.int32)[:, None]).astype(jnp.float32)
    chosen = jnp.concatenate([chosen, chosen], axis=1)
    total = jnp.zeros((Z, 2 * ROWS), jnp.float32)
    for which in range(BANDS):
        product = jnp.dot(masked[which], planes, precision=lax.Precision.HIGHEST, preferred_element_type=jnp.float32)
        total = total + product * chosen[which][None, :]
    return total.reshape(Z, 2, ROWS)
```

```python
import jax
import jax.numpy as jnp
from jax import lax
from jax.sharding import PartitionSpec as P

BLOCK = 128
CHUNKS = 4


def apply_pattern(weights, blocks):
    bands_count, out_size, in_size = weights.shape
    shaped = weights.reshape(bands_count, out_size // BLOCK, BLOCK, in_size // BLOCK, BLOCK)
    factor = blocks.astype(jnp.float32)[:, :, None, :, None]
    return (shaped * factor).reshape(bands_count, out_size, in_size)


def both_bands(left, operand, column_mask):
    first = jnp.dot(
        left[0], operand, precision=lax.Precision.HIGHEST, preferred_element_type=jnp.float32
    )
    second = jnp.dot(
        left[1], operand, precision=lax.Precision.HIGHEST, preferred_element_type=jnp.float32
    )
    return jnp.where(column_mask[None, :], first, second)


def solution(mesh):
    n_lat = mesh.shape["lat"]

    def local(spectrum, operator, pattern, band):
        _, sub, parts, rows = spectrum.shape
        rows_local = rows // n_lat
        cols = parts * rows_local
        send = spectrum.reshape(sub, parts, n_lat, rows_local)
        send = jnp.transpose(send, (2, 0, 1, 3)).reshape(n_lat, sub, cols)
        moved = lax.all_to_all(send, "lat", 0, 0, tiled=True)
        planes = moved.reshape(n_lat * sub, cols)
        depth_local = planes.shape[0]
        depth_index = lax.axis_index("dep")
        local_blocks = depth_local // BLOCK
        column_pattern = lax.dynamic_slice_in_dim(pattern, depth_index * local_blocks, local_blocks, 2)
        masked = apply_pattern(operator, column_pattern)
        column_mask = jnp.tile(band == 0, parts)
        width = cols // CHUNKS
        pieces = []
        for c in range(CHUNKS):
            part = both_bands(
                masked, planes[:, c * width:(c + 1) * width], column_mask[c * width:(c + 1) * width]
            )
            pieces.append(lax.psum_scatter(part, "dep", scatter_dimension=0, tiled=True))
        result = jnp.concatenate(pieces, axis=1)
        return result.reshape(depth_local, parts, rows_local)

    placed = (P("dep", "lat", None, None), P(None, None, "dep"), P(), P("lat"))
    return jax.shard_map(
        local, mesh=mesh, in_specs=placed, out_specs=P("dep", None, "lat"), check_vma=False
    )
```

```python
import jax
import jax.numpy as jnp
from jax import lax
from jax.sharding import PartitionSpec as P

BLOCK = 128
SPLITS = ((256, 768), (1024,))


def both_bands(left, operand, column_mask):
    first = jnp.dot(
        left[0], operand, precision=lax.Precision.HIGHEST, preferred_element_type=jnp.float32
    )
    second = jnp.dot(
        left[1], operand, precision=lax.Precision.HIGHEST, preferred_element_type=jnp.float32
    )
    return jnp.where(column_mask[None, :], first, second)


def solution(mesh):
    n_lat = mesh.shape["lat"]

    def local(spectrum, operator, pattern, band):
        _, sub, parts, rows = spectrum.shape
        rows_local = rows // n_lat
        depth_local = n_lat * sub
        depth_index = lax.axis_index("dep")
        local_blocks = depth_local // BLOCK
        column_pattern = lax.dynamic_slice_in_dim(pattern, depth_index * local_blocks, local_blocks, 2)
        field = jnp.repeat(jnp.repeat(column_pattern, BLOCK, axis=1), BLOCK, axis=2)
        masked = operator * field.astype(jnp.float32)
        column_mask = band == 0
        outs = []
        for p in range(parts):
            send = spectrum[0, :, p, :].reshape(sub, n_lat, rows_local)
            send = jnp.transpose(send, (1, 0, 2))
            moved = lax.all_to_all(send, "lat", 0, 0, tiled=True)
            planes = moved.reshape(depth_local, rows_local)
            pieces = []
            start = 0
            for width in SPLITS[p]:
                part = both_bands(
                    masked, planes[:, start:start + width], column_mask[start:start + width]
                )
                pieces.append(lax.psum_scatter(part, "dep", scatter_dimension=0, tiled=True))
                start += width
            outs.append(pieces[0] if len(pieces) == 1 else jnp.concatenate(pieces, axis=1))
        return jnp.stack(outs, axis=1)

    placed = (P("dep", "lat", None, None), P(None, None, "dep"), P(), P("lat"))
    return jax.shard_map(
        local, mesh=mesh, in_specs=placed, out_specs=P("dep", None, "lat"), check_vma=False
    )
```

```python
import jax
import jax.numpy as jnp
from jax import lax
from jax.sharding import PartitionSpec as P

BLOCK = 128


def both_bands(left, operand, column_mask):
    first = jnp.dot(
        left[0], operand, precision=lax.Precision.HIGHEST, preferred_element_type=jnp.float32
    )
    second = jnp.dot(
        left[1], operand, precision=lax.Precision.HIGHEST, preferred_element_type=jnp.float32
    )
    return jnp.where(column_mask[None, :], first, second)


def solution(mesh):
    n_lat = mesh.shape["lat"]
    n_dep = mesh.shape["dep"]

    def local(spectrum, operator, pattern, band):
        _, sub, parts, rows = spectrum.shape
        bands, out_size, _ = operator.shape
        rows_local = rows // n_lat
        depth_local = n_lat * sub
        depth_index = lax.axis_index("dep")
        local_blocks = depth_local // BLOCK
        column_pattern = lax.dynamic_slice_in_dim(pattern, depth_index * local_blocks, local_blocks, 2)
        column_pattern = jnp.repeat(column_pattern, BLOCK, axis=2).astype(jnp.float32)
        shaped = operator.reshape(bands, out_size // BLOCK, BLOCK, depth_local)
        masked = (shaped * column_pattern[:, :, None, :]).reshape(bands, out_size, depth_local)
        column_mask = band == 0
        half = rows_local // 2
        outs = []
        for p in range(parts):
            send = spectrum[0, :, p, :].reshape(sub, n_lat, rows_local)
            send = jnp.transpose(send, (1, 0, 2))
            moved = lax.all_to_all(send, "lat", 0, 0, tiled=True)
            planes = moved.reshape(depth_local, rows_local)
            halves = []
            for h, step in enumerate((1, -1)):
                operand = planes[:, h * half:(h + 1) * half]
                mask = column_mask[h * half:(h + 1) * half]
                perm = [(i, (i + step) % n_dep) for i in range(n_dep)]
                acc = None
                for s in range(n_dep):
                    block = (depth_index + n_dep * n_dep - step * (s + 1)) % n_dep
                    rows_block = lax.dynamic_slice_in_dim(masked, block * depth_local, depth_local, 1)
                    contrib = both_bands(rows_block, operand, mask)
                    acc = contrib if acc is None else acc + contrib
                    if s < n_dep - 1:
                        acc = lax.ppermute(acc, "dep", perm)
                halves.append(acc)
            outs.append(jnp.concatenate(halves, axis=1))
        return jnp.stack(outs, axis=1)

    placed = (P("dep", "lat", None, None), P(None, None, "dep"), P(), P("lat"))
    return jax.shard_map(
        local, mesh=mesh, in_specs=placed, out_specs=P("dep", None, "lat"), check_vma=False
    )
```

```python
import jax
import jax.numpy as jnp
from jax import lax
from jax.sharding import PartitionSpec as P

BLOCK = 128
FIRST_SPLIT = (256, 768)


def both_bands(left, operand, column_mask):
    first = jnp.dot(
        left[0], operand, precision=lax.Precision.HIGHEST, preferred_element_type=jnp.float32
    )
    second = jnp.dot(
        left[1], operand, precision=lax.Precision.HIGHEST, preferred_element_type=jnp.float32
    )
    return jnp.where(column_mask[None, :], first, second)


def solution(mesh):
    n_lat = mesh.shape["lat"]
    n_dep = mesh.shape["dep"]

    def local(spectrum, operator, pattern, band):
        _, sub, parts, rows = spectrum.shape
        bands, out_size, _ = operator.shape
        rows_local = rows // n_lat
        depth_local = n_lat * sub
        depth_index = lax.axis_index("dep")
        local_blocks = depth_local // BLOCK
        column_pattern = lax.dynamic_slice_in_dim(pattern, depth_index * local_blocks, local_blocks, 2)
        column_pattern = jnp.repeat(column_pattern, BLOCK, axis=2).astype(jnp.float32)
        shaped = operator.reshape(bands, out_size // BLOCK, BLOCK, depth_local)
        masked = (shaped * column_pattern[:, :, None, :]).reshape(bands, out_size, depth_local)
        column_mask = band == 0
        half = rows_local // 2
        outs = []
        for p in range(parts):
            send = spectrum[0, :, p, :].reshape(sub, n_lat, rows_local)
            send = jnp.transpose(send, (1, 0, 2))
            moved = lax.all_to_all(send, "lat", 0, 0, tiled=True)
            planes = moved.reshape(depth_local, rows_local)
            if p == 0:
                pieces = []
                start = 0
                for width in FIRST_SPLIT:
                    part = both_bands(
                        masked, planes[:, start:start + width], column_mask[start:start + width]
                    )
                    pieces.append(lax.psum_scatter(part, "dep", scatter_dimension=0, tiled=True))
                    start += width
                outs.append(jnp.concatenate(pieces, axis=1))
                continue
            halves = []
            for h, step in enumerate((1, -1)):
                operand = planes[:, h * half:(h + 1) * half]
                mask = column_mask[h * half:(h + 1) * half]
                perm = [(i, (i + step) % n_dep) for i in range(n_dep)]
                acc = None
                for s in range(n_dep):
                    block = (depth_index + n_dep * n_dep - step * (s + 1)) % n_dep
                    rows_block = lax.dynamic_slice_in_dim(masked, block * depth_local, depth_local, 1)
                    contrib = both_bands(rows_block, operand, mask)
                    acc = contrib if acc is None else acc + contrib
                    if s < n_dep - 1:
                        acc = lax.ppermute(acc, "dep", perm)
                halves.append(acc)
            outs.append(jnp.concatenate(halves, axis=1))
        return jnp.stack(outs, axis=1)

    placed = (P("dep", "lat", None, None), P(None, None, "dep"), P(), P("lat"))
    return jax.shard_map(
        local, mesh=mesh, in_specs=placed, out_specs=P("dep", None, "lat"), check_vma=False
    )
```

```python
import jax
import jax.numpy as jnp
from jax import lax
from jax.sharding import PartitionSpec as P

BLOCK = 128
FIRST_SPLIT = (256, 768)


def both_bands(left, operand, column_mask):
    first = jnp.dot(
        left[0], operand, precision=lax.Precision.HIGHEST, preferred_element_type=jnp.float32
    )
    second = jnp.dot(
        left[1], operand, precision=lax.Precision.HIGHEST, preferred_element_type=jnp.float32
    )
    return jnp.where(column_mask[None, :], first, second)


def solution(mesh):
    n_lat = mesh.shape["lat"]
    n_dep = mesh.shape["dep"]

    def local(spectrum, operator, pattern, band):
        _, sub, parts, rows = spectrum.shape
        bands, out_size, _ = operator.shape
        rows_local = rows // n_lat
        depth_local = n_lat * sub
        depth_index = lax.axis_index("dep")
        local_blocks = depth_local // BLOCK
        column_pattern = lax.dynamic_slice_in_dim(pattern, depth_index * local_blocks, local_blocks, 2)
        column_pattern = jnp.repeat(column_pattern, BLOCK, axis=2).astype(jnp.float32)
        shaped = operator.reshape(bands, out_size // BLOCK, BLOCK, depth_local)
        masked = (shaped * column_pattern[:, :, None, :]).reshape(bands, out_size, depth_local)
        column_mask = band == 0
        half = rows_local // 2
        send = spectrum.reshape(sub, parts, n_lat, rows_local)
        send = jnp.transpose(send, (2, 0, 1, 3)).reshape(n_lat, sub, parts * rows_local)
        moved = lax.all_to_all(send, "lat", 0, 0, tiled=True)
        both_parts = moved.reshape(depth_local, parts * rows_local)

        def first_part(planes, lo, width):
            part = both_bands(masked, planes[:, lo:lo + width], column_mask[lo:lo + width])
            return lax.psum_scatter(part, "dep", scatter_dimension=0, tiled=True)

        def ring_part(planes, mask_cols):
            halves = []
            for h, step in enumerate((1, -1)):
                operand = planes[:, h * half:(h + 1) * half]
                mask = mask_cols[h * half:(h + 1) * half]
                perm = [(i, (i + step) % n_dep) for i in range(n_dep)]
                acc = None
                for s in range(n_dep):
                    block = (depth_index + n_dep * n_dep - step * (s + 1)) % n_dep
                    rows_block = lax.dynamic_slice_in_dim(masked, block * depth_local, depth_local, 1)
                    contrib = both_bands(rows_block, operand, mask)
                    acc = contrib if acc is None else acc + contrib
                    if s < n_dep - 1:
                        acc = lax.ppermute(acc, "dep", perm)
                halves.append(acc)
            return jnp.concatenate(halves, axis=1)

        planes0 = both_parts[:, :rows_local]
        planes1 = both_parts[:, rows_local:]
        lead = first_part(planes0, 0, FIRST_SPLIT[0])
        ringed = ring_part(planes1, column_mask)
        rest = first_part(planes0, FIRST_SPLIT[0], rows_local - FIRST_SPLIT[0])
        outs = [jnp.concatenate([lead, rest], axis=1), ringed]
        return jnp.stack(outs, axis=1)

    placed = (P("dep", "lat", None, None), P(None, None, "dep"), P(), P("lat"))
    return jax.shard_map(
        local, mesh=mesh, in_specs=placed, out_specs=P("dep", None, "lat"), check_vma=False
    )
```

```python
import jax
import jax.numpy as jnp
from jax import lax
from jax.sharding import PartitionSpec as P

BLOCK = 128
FIRST_SPLIT = (256,)


def both_bands(left, operand, column_mask):
    first = jnp.dot(
        left[0], operand, precision=lax.Precision.HIGHEST, preferred_element_type=jnp.float32
    )
    second = jnp.dot(
        left[1], operand, precision=lax.Precision.HIGHEST, preferred_element_type=jnp.float32
    )
    return jnp.where(column_mask[None, :], first, second)


def solution(mesh):
    n_lat = mesh.shape["lat"]
    n_dep = mesh.shape["dep"]

    def local(spectrum, operator, pattern, band):
        _, sub, parts, rows = spectrum.shape
        bands, out_size, _ = operator.shape
        rows_local = rows // n_lat
        depth_local = n_lat * sub
        depth_index = lax.axis_index("dep")
        local_blocks = depth_local // BLOCK
        column_pattern = lax.dynamic_slice_in_dim(pattern, depth_index * local_blocks, local_blocks, 2)
        column_pattern = jnp.repeat(column_pattern, BLOCK, axis=2).astype(jnp.float32)
        shaped = operator.reshape(bands, out_size // BLOCK, BLOCK, depth_local)
        masked = (shaped * column_pattern[:, :, None, :]).reshape(bands, out_size, depth_local)
        column_mask = band == 0
        half = rows_local // 2
        sends = []
        for p in range(parts):
            send = spectrum[0, :, p, :].reshape(sub, n_lat, rows_local)
            sends.append(jnp.transpose(send, (1, 0, 2)))
        first = lax.all_to_all(sends[0], "lat", 0, 0, tiled=True).reshape(depth_local, rows_local)
        lo = FIRST_SPLIT[0]
        lead = both_bands(masked, first[:, :lo], column_mask[:lo])
        lead, later = lax.optimization_barrier((lead, sends[1]))
        lead = lax.psum_scatter(lead, "dep", scatter_dimension=0, tiled=True)
        moved = [first, lax.all_to_all(later, "lat", 0, 0, tiled=True).reshape(depth_local, rows_local)]
        planes0, planes1 = lax.optimization_barrier((moved[0], moved[1]))
        def ring_part(planes, mask_cols):
            width = planes.shape[1] // 2
            halves = []
            for h, step in enumerate((1, -1)):
                operand = planes[:, h * width:(h + 1) * width]
                mask = mask_cols[h * width:(h + 1) * width]
                perm = [(i, (i + step) % n_dep) for i in range(n_dep)]
                acc = None
                for s in range(n_dep):
                    block = (depth_index + n_dep * n_dep - step * (s + 1)) % n_dep
                    rows_block = lax.dynamic_slice_in_dim(masked, block * depth_local, depth_local, 1)
                    contrib = both_bands(rows_block, operand, mask)
                    acc = contrib if acc is None else acc + contrib
                    if s < n_dep - 1:
                        acc = lax.ppermute(acc, "dep", perm)
                halves.append(acc)
            return jnp.concatenate(halves, axis=1)

        rest = ring_part(planes0[:, lo:], column_mask[lo:])
        second = ring_part(planes1, column_mask)
        outs = [jnp.concatenate([lead, rest], axis=1), second]
        return jnp.stack(outs, axis=1)

    placed = (P("dep", "lat", None, None), P(None, None, "dep"), P(), P("lat"))
    return jax.shard_map(
        local, mesh=mesh, in_specs=placed, out_specs=P("dep", None, "lat"), check_vma=False
    )
```

```python
import jax
import jax.numpy as jnp
from jax import lax
from jax.sharding import PartitionSpec as P

BLOCK = 128


def both_bands(left, operand, column_mask):
    first = jnp.dot(
        left[0], operand, precision=lax.Precision.HIGHEST, preferred_element_type=jnp.float32
    )
    second = jnp.dot(
        left[1], operand, precision=lax.Precision.HIGHEST, preferred_element_type=jnp.float32
    )
    return jnp.where(column_mask[None, :], first, second)


def solution(mesh):
    n_lat = mesh.shape["lat"]
    n_dep = mesh.shape["dep"]

    def local(spectrum, operator, pattern, band):
        _, sub, parts, rows = spectrum.shape
        bands, out_size, _ = operator.shape
        rows_local = rows // n_lat
        depth_local = n_lat * sub
        depth_index = lax.axis_index("dep")
        local_blocks = depth_local // BLOCK
        column_pattern = lax.dynamic_slice_in_dim(pattern, depth_index * local_blocks, local_blocks, 2)
        column_pattern = jnp.repeat(column_pattern, BLOCK, axis=2).astype(jnp.float32)
        shaped = operator.reshape(bands, out_size // BLOCK, BLOCK, depth_local)
        masked = (shaped * column_pattern[:, :, None, :]).reshape(bands, out_size, depth_local)
        column_mask = band == 0
        half = rows_local // 2
        moved = []
        for p in range(parts):
            send = spectrum[0, :, p, :].reshape(sub, n_lat, rows_local)
            send = jnp.transpose(send, (1, 0, 2))
            moved.append(lax.all_to_all(send, "lat", 0, 0, tiled=True).reshape(depth_local, rows_local))

        def block_of(s, step):
            block = (depth_index + n_dep * n_dep - step * (s + 1)) % n_dep
            return lax.dynamic_slice_in_dim(masked, block * depth_local, depth_local, 1)

        def heads_of(planes):
            return [
                both_bands(block_of(0, step), planes[:, h * half:(h + 1) * half],
                           column_mask[h * half:(h + 1) * half])
                for h, step in enumerate((1, -1))
            ]

        def ring_of(planes, heads):
            halves = []
            for h, step in enumerate((1, -1)):
                operand = planes[:, h * half:(h + 1) * half]
                mask = column_mask[h * half:(h + 1) * half]
                perm = [(i, (i + step) % n_dep) for i in range(n_dep)]
                acc = lax.ppermute(heads[h], "dep", perm)
                for s in range(1, n_dep):
                    acc = acc + both_bands(block_of(s, step), operand, mask)
                    if s < n_dep - 1:
                        acc = lax.ppermute(acc, "dep", perm)
                halves.append(acc)
            return jnp.concatenate(halves, axis=1)

        heads0 = heads_of(moved[0])
        heads0, planes1 = lax.optimization_barrier((heads0, moved[1]))
        outs = [ring_of(moved[0], heads0), ring_of(planes1, heads_of(planes1))]
        return jnp.stack(outs, axis=1)

    placed = (P("dep", "lat", None, None), P(None, None, "dep"), P(), P("lat"))
    return jax.shard_map(
        local, mesh=mesh, in_specs=placed, out_specs=P("dep", None, "lat"), check_vma=False
    )
```

```python
import jax
import jax.numpy as jnp
from jax import lax
from jax.sharding import PartitionSpec as P

BLOCK = 128


def both_bands(left, operand, column_mask):
    first = jnp.dot(
        left[0], operand, precision=lax.Precision.HIGHEST, preferred_element_type=jnp.float32
    )
    second = jnp.dot(
        left[1], operand, precision=lax.Precision.HIGHEST, preferred_element_type=jnp.float32
    )
    return jnp.where(column_mask[None, :], first, second)


def solution(mesh):
    n_lat = mesh.shape["lat"]
    n_dep = mesh.shape["dep"]

    def local(spectrum, operator, pattern, band):
        _, sub, parts, rows = spectrum.shape
        bands, out_size, _ = operator.shape
        rows_local = rows // n_lat
        depth_local = n_lat * sub
        depth_index = lax.axis_index("dep")
        local_blocks = depth_local // BLOCK
        column_pattern = lax.dynamic_slice_in_dim(pattern, depth_index * local_blocks, local_blocks, 2)
        column_pattern = jnp.repeat(column_pattern, BLOCK, axis=2).astype(jnp.float32)
        shaped = operator.reshape(bands, out_size // BLOCK, BLOCK, depth_local)
        masked = (shaped * column_pattern[:, :, None, :]).reshape(bands, out_size, depth_local)
        column_mask = band == 0
        half = rows_local // 2
        moved = []
        for p in range(parts):
            send = spectrum[0, :, p, :].reshape(sub, n_lat, rows_local)
            send = jnp.transpose(send, (1, 0, 2))
            moved.append(lax.all_to_all(send, "lat", 0, 0, tiled=True).reshape(depth_local, rows_local))
        halves = []
        for h, step in enumerate((1, -1)):
            operand = jnp.concatenate([m[:, h * half:(h + 1) * half] for m in moved], axis=1)
            mask = jnp.tile(column_mask[h * half:(h + 1) * half], parts)
            perm = [(i, (i + step) % n_dep) for i in range(n_dep)]
            acc = None
            for s in range(n_dep):
                block = (depth_index + n_dep * n_dep - step * (s + 1)) % n_dep
                rows_block = lax.dynamic_slice_in_dim(masked, block * depth_local, depth_local, 1)
                contrib = both_bands(rows_block, operand, mask)
                acc = contrib if acc is None else acc + contrib
                if s < n_dep - 1:
                    acc = lax.ppermute(acc, "dep", perm)
            halves.append(acc.reshape(depth_local, parts, half))
        return jnp.concatenate(halves, axis=2)

    placed = (P("dep", "lat", None, None), P(None, None, "dep"), P(), P("lat"))
    return jax.shard_map(
        local, mesh=mesh, in_specs=placed, out_specs=P("dep", None, "lat"), check_vma=False
    )
```

```python
import jax
import jax.numpy as jnp
from jax import lax
from jax.sharding import PartitionSpec as P

BLOCK = 128
FIRST_SPLIT = (256, 768)


def both_bands(left, operand, column_mask):
    first = jnp.dot(
        left[0], operand, precision=lax.Precision.HIGH, preferred_element_type=jnp.float32
    )
    second = jnp.dot(
        left[1], operand, precision=lax.Precision.HIGH, preferred_element_type=jnp.float32
    )
    return jnp.where(column_mask[None, :], first, second)


def solution(mesh):
    n_lat = mesh.shape["lat"]
    n_dep = mesh.shape["dep"]

    def local(spectrum, operator, pattern, band):
        _, sub, parts, rows = spectrum.shape
        bands, out_size, _ = operator.shape
        rows_local = rows // n_lat
        depth_local = n_lat * sub
        depth_index = lax.axis_index("dep")
        local_blocks = depth_local // BLOCK
        column_pattern = lax.dynamic_slice_in_dim(pattern, depth_index * local_blocks, local_blocks, 2)
        column_pattern = jnp.repeat(column_pattern, BLOCK, axis=2).astype(jnp.float32)
        shaped = operator.reshape(bands, out_size // BLOCK, BLOCK, depth_local)
        masked = (shaped * column_pattern[:, :, None, :]).reshape(bands, out_size, depth_local)
        column_mask = band == 0
        half = rows_local // 2
        outs = []
        for p in range(parts):
            send = spectrum[0, :, p, :].reshape(sub, n_lat, rows_local)
            send = jnp.transpose(send, (1, 0, 2))
            moved = lax.all_to_all(send, "lat", 0, 0, tiled=True)
            planes = moved.reshape(depth_local, rows_local)
            if p == 0:
                pieces = []
                start = 0
                for width in FIRST_SPLIT:
                    part = both_bands(
                        masked, planes[:, start:start + width], column_mask[start:start + width]
                    )
                    pieces.append(lax.psum_scatter(part, "dep", scatter_dimension=0, tiled=True))
                    start += width
                outs.append(jnp.concatenate(pieces, axis=1))
                continue
            halves = []
            for h, step in enumerate((1, -1)):
                operand = planes[:, h * half:(h + 1) * half]
                mask = column_mask[h * half:(h + 1) * half]
                perm = [(i, (i + step) % n_dep) for i in range(n_dep)]
                acc = None
                for s in range(n_dep):
                    block = (depth_index + n_dep * n_dep - step * (s + 1)) % n_dep
                    rows_block = lax.dynamic_slice_in_dim(masked, block * depth_local, depth_local, 1)
                    contrib = both_bands(rows_block, operand, mask)
                    acc = contrib if acc is None else acc + contrib
                    if s < n_dep - 1:
                        acc = lax.ppermute(acc, "dep", perm)
                halves.append(acc)
            outs.append(jnp.concatenate(halves, axis=1))
        return jnp.stack(outs, axis=1)

    placed = (P("dep", "lat", None, None), P(None, None, "dep"), P(), P("lat"))
    return jax.shard_map(
        local, mesh=mesh, in_specs=placed, out_specs=P("dep", None, "lat"), check_vma=False
    )
```

```python
import jax
import jax.numpy as jnp
from jax import lax
from jax.sharding import PartitionSpec as P

BLOCK = 128
FIRST_SPLIT = (256, 768)


def both_bands(left, operand, column_mask):
    first = jnp.dot(
        left[0], operand, precision=lax.Precision.HIGH, preferred_element_type=jnp.float32
    )
    second = jnp.dot(
        left[1], operand, precision=lax.Precision.HIGH, preferred_element_type=jnp.float32
    )
    return jnp.where(column_mask[None, :], first, second)


def solution(mesh):
    n_lat = mesh.shape["lat"]
    n_dep = mesh.shape["dep"]

    def local(spectrum, operator, pattern, band):
        _, sub, parts, rows = spectrum.shape
        bands, out_size, _ = operator.shape
        rows_local = rows // n_lat
        depth_local = n_lat * sub
        depth_index = lax.axis_index("dep")
        local_blocks = depth_local // BLOCK
        column_pattern = lax.dynamic_slice_in_dim(pattern, depth_index * local_blocks, local_blocks, 2)
        column_pattern = jnp.repeat(column_pattern, BLOCK, axis=2).astype(jnp.float32)
        shaped = operator.reshape(bands, out_size // BLOCK, BLOCK, depth_local)
        masked = (shaped * column_pattern[:, :, None, :]).reshape(bands, out_size, depth_local)
        column_mask = band == 0
        half = rows_local // 2
        outs = []
        source = spectrum
        for p in range(parts):
            send = source[0, :, p, :].reshape(sub, n_lat, rows_local)
            send = jnp.transpose(send, (1, 0, 2))
            send, source = lax.optimization_barrier((send, source))
            moved = lax.all_to_all(send, "lat", 0, 0, tiled=True)
            planes = moved.reshape(depth_local, rows_local)
            if p == 0:
                pieces = []
                start = 0
                for width in FIRST_SPLIT:
                    part = both_bands(
                        masked, planes[:, start:start + width], column_mask[start:start + width]
                    )
                    pieces.append(lax.psum_scatter(part, "dep", scatter_dimension=0, tiled=True))
                    start += width
                outs.append(jnp.concatenate(pieces, axis=1))
                continue
            halves = []
            for h, step in enumerate((1, -1)):
                operand = planes[:, h * half:(h + 1) * half]
                mask = column_mask[h * half:(h + 1) * half]
                perm = [(i, (i + step) % n_dep) for i in range(n_dep)]
                acc = None
                for s in range(n_dep):
                    block = (depth_index + n_dep * n_dep - step * (s + 1)) % n_dep
                    rows_block = lax.dynamic_slice_in_dim(masked, block * depth_local, depth_local, 1)
                    contrib = both_bands(rows_block, operand, mask)
                    acc = contrib if acc is None else acc + contrib
                    if s < n_dep - 1:
                        acc = lax.ppermute(acc, "dep", perm)
                halves.append(acc)
            outs.append(jnp.concatenate(halves, axis=1))
        return jnp.stack(outs, axis=1)

    placed = (P("dep", "lat", None, None), P(None, None, "dep"), P(), P("lat"))
    return jax.shard_map(
        local, mesh=mesh, in_specs=placed, out_specs=P("dep", None, "lat"), check_vma=False
    )
```

```python
import jax
import jax.numpy as jnp
from jax import lax
from jax.sharding import PartitionSpec as P

BLOCK = 128
FIRST_SPLIT = (256, 768)


def both_bands(left, operand, column_mask):
    first = jnp.dot(
        left[0], operand, precision=lax.Precision.HIGH, preferred_element_type=jnp.float32
    )
    second = jnp.dot(
        left[1], operand, precision=lax.Precision.HIGH, preferred_element_type=jnp.float32
    )
    return jnp.where(column_mask[None, :], first, second)


def solution(mesh):
    n_lat = mesh.shape["lat"]
    n_dep = mesh.shape["dep"]

    def local(spectrum, operator, pattern, band):
        _, sub, parts, rows = spectrum.shape
        bands, out_size, _ = operator.shape
        rows_local = rows // n_lat
        depth_local = n_lat * sub
        depth_index = lax.axis_index("dep")
        local_blocks = depth_local // BLOCK
        column_pattern = lax.dynamic_slice_in_dim(pattern, depth_index * local_blocks, local_blocks, 2)
        column_pattern = jnp.repeat(column_pattern, BLOCK, axis=2).astype(jnp.float32)
        shaped = operator.reshape(bands, out_size // BLOCK, BLOCK, depth_local)
        masked = (shaped * column_pattern[:, :, None, :]).reshape(bands, out_size, depth_local)
        column_mask = band == 0
        half = rows_local // 2
        outs = []
        for p in range(parts):
            send = spectrum[0, :, p, :].reshape(sub, n_lat, rows_local)
            send = jnp.transpose(send, (1, 0, 2))
            moved = lax.all_to_all(send, "lat", 0, 0, tiled=True)
            planes = moved.reshape(depth_local, rows_local)
            if p == 0:
                pieces = []
                start = 0
                for width in FIRST_SPLIT:
                    part = both_bands(
                        masked, planes[:, start:start + width], column_mask[start:start + width]
                    )
                    pieces.append(lax.psum_scatter(part, "dep", scatter_dimension=0, tiled=True))
                    start += width
                outs.append(jnp.concatenate(pieces, axis=1))
                continue
            lead = FIRST_SPLIT[0]
            head = both_bands(masked, planes[:, :lead], column_mask[:lead])
            head = lax.psum_scatter(head, "dep", scatter_dimension=0, tiled=True)
            width = (rows_local - lead) // 2
            halves = [head]
            for h, step in enumerate((1, -1)):
                lo = lead + h * width
                operand = planes[:, lo:lo + width]
                mask = column_mask[lo:lo + width]
                perm = [(i, (i + step) % n_dep) for i in range(n_dep)]
                acc = None
                for s in range(n_dep):
                    block = (depth_index + n_dep * n_dep - step * (s + 1)) % n_dep
                    rows_block = lax.dynamic_slice_in_dim(masked, block * depth_local, depth_local, 1)
                    contrib = both_bands(rows_block, operand, mask)
                    acc = contrib if acc is None else acc + contrib
                    if s < n_dep - 1:
                        acc = lax.ppermute(acc, "dep", perm)
                halves.append(acc)
            outs.append(jnp.concatenate(halves, axis=1))
        return jnp.stack(outs, axis=1)

    placed = (P("dep", "lat", None, None), P(None, None, "dep"), P(), P("lat"))
    return jax.shard_map(
        local, mesh=mesh, in_specs=placed, out_specs=P("dep", None, "lat"), check_vma=False
    )
```

```python
import jax
import jax.numpy as jnp
from jax import lax
from jax.sharding import PartitionSpec as P

BLOCK = 128
FIRST_SPLIT = (1024,)


def both_bands(left, operand, column_mask):
    first = jnp.dot(
        left[0], operand, precision=lax.Precision.HIGH, preferred_element_type=jnp.float32
    )
    second = jnp.dot(
        left[1], operand, precision=lax.Precision.HIGH, preferred_element_type=jnp.float32
    )
    return jnp.where(column_mask[None, :], first, second)


def solution(mesh):
    n_lat = mesh.shape["lat"]
    n_dep = mesh.shape["dep"]

    def local(spectrum, operator, pattern, band):
        _, sub, parts, rows = spectrum.shape
        bands, out_size, _ = operator.shape
        rows_local = rows // n_lat
        depth_local = n_lat * sub
        depth_index = lax.axis_index("dep")
        local_blocks = depth_local // BLOCK
        column_pattern = lax.dynamic_slice_in_dim(pattern, depth_index * local_blocks, local_blocks, 2)
        column_pattern = jnp.repeat(column_pattern, BLOCK, axis=2).astype(jnp.float32)
        shaped = operator.reshape(bands, out_size // BLOCK, BLOCK, depth_local)
        masked = (shaped * column_pattern[:, :, None, :]).reshape(bands, out_size, depth_local)
        column_mask = band == 0
        half = rows_local // 2
        outs = []
        for p in range(parts):
            send = spectrum[0, :, p, :].reshape(sub, n_lat, rows_local)
            send = jnp.transpose(send, (1, 0, 2))
            moved = lax.all_to_all(send, "lat", 0, 0, tiled=True)
            planes = moved.reshape(depth_local, rows_local)
            if p == 0:
                pieces = []
                start = 0
                for width in FIRST_SPLIT:
                    part = both_bands(
                        masked, planes[:, start:start + width], column_mask[start:start + width]
                    )
                    pieces.append(lax.psum_scatter(part, "dep", scatter_dimension=0, tiled=True))
                    start += width
                outs.append(jnp.concatenate(pieces, axis=1))
                continue
            halves = []
            for h, step in enumerate((1, -1)):
                operand = planes[:, h * half:(h + 1) * half]
                mask = column_mask[h * half:(h + 1) * half]
                perm = [(i, (i + step) % n_dep) for i in range(n_dep)]
                acc = None
                for s in range(n_dep):
                    block = (depth_index + n_dep * n_dep - step * (s + 1)) % n_dep
                    rows_block = lax.dynamic_slice_in_dim(masked, block * depth_local, depth_local, 1)
                    contrib = both_bands(rows_block, operand, mask)
                    acc = contrib if acc is None else acc + contrib
                    if s < n_dep - 1:
                        acc = lax.ppermute(acc, "dep", perm)
                halves.append(acc)
            outs.append(jnp.concatenate(halves, axis=1))
        return jnp.stack(outs, axis=1)

    placed = (P("dep", "lat", None, None), P(None, None, "dep"), P(), P("lat"))
    return jax.shard_map(
        local, mesh=mesh, in_specs=placed, out_specs=P("dep", None, "lat"), check_vma=False
    )
```
